256 devices in a mesh: rows: 64 (over x, z, core), rep: 4 (over y).
Axes of the slice: x: 4, y: 4, z: 8, core: 2. Of those that a mesh axis runs over, the one named last changes fastest.
Arguments:
- a_vals: float32 [4, 512, 4, 128, 128], P('rep', 'rows'), may hold values from -0.25 to 0.25
- a_tgt: int32 [4, 512, 4], P('rep', 'rows'), may hold values from 0 to 9, all different within a row
- b_vals: float32 [512, 128, 12, 128], P(('rows', 'rep')), may hold values from -6 to 6
- b_cols: int32 [64, 12], P('rows'), may hold values from 0 to 511, as said below
- c_cols: int32 [512, 8], P(('rows', 'rep')), may hold values from 0 to 511, as said below
- c_count: int32 [512], P(('rows', 'rep')), may hold values from 1 to 8, 2560 in all
Outputs:
- c_vals: float32 [512, 8, 128, 128], P(('rows', 'rep'))
- row_start: int32 [512], P(('rows', 'rep'))
The draws below stay inside these ranges and needn't reach their ends.
Inputs may be any that keep to these rules, and one draw needn't show every extreme that they name: `b_cols`: row g holds 12 distinct columns, each (g * 8 + 8 // 2 - 8 + o) mod 512 with o in 0 to 15. `c_cols`: row i holds 8 distinct columns, each ((i // 8) * 8 + 8 // 2 - 2 * 8 - 8 + o) mod 512 with o in 0 to 47. `a_tgt`: the 4 targets of one quarter and block column are distinct. `c_count`: the counts sum to 2560.
All inputs are finite; a program needn't handle non-finite values. No bound on the sum of `c_count` on one device may be relied on, other than what follows from the above.
Results may differ from the reference program's by a relative error of at most 0.0003.
Values sent between devices are 32-bit elements; how exact they have to be, the bound alone decides.
No kernel may reach another device: no remote copies, remote signals or barrier semaphores. Data moves between devices by JAX's collectives and lax.ppermute only.
A program may use at most 128 MiB of HBM per device.

```python
import math
import jax
import jax.numpy as jnp
import numpy as np
from jax import lax

BS = 128
REACH = 2
ASL_DEV = 4
BSL = 12
CSL = 8
HB = 8
CAVG = 5
GR = 8
NG = 64
NB = 512
TG = 10
N_REP = 4


def draw_b_cols(key, part):
    window_cols = 2 * HB
    scores = jax.random.randint(key, (NG, window_cols), 0, 4096, dtype=jnp.int32) * window_cols + jnp.arange(window_cols, dtype=jnp.int32)[None, :]
    picked = jnp.argsort(scores, axis=1)[:, :BSL].astype(jnp.int32)
    first_col = jnp.arange(NG, dtype=jnp.int32) * GR + GR // 2 - HB
    return ((first_col[:, None] + picked) % NB).astype(jnp.int32)


def draw_c_cols(key, part):
    window_cols = 2 * REACH * GR + 2 * HB
    scores = jax.random.randint(key, (NB, window_cols), 0, 4096, dtype=jnp.int32) * window_cols + jnp.arange(window_cols, dtype=jnp.int32)[None, :]
    picked = jnp.argsort(scores, axis=1)[:, :CSL].astype(jnp.int32)
    row_group = jnp.arange(NB, dtype=jnp.int32) // GR
    first_col = row_group * GR + GR // 2 - REACH * GR - HB
    return ((first_col[:, None] + picked) % NB).astype(jnp.int32)


def shard_levels(rng, extent, shards, smallest, high):
    def one(axis_at, blocks):
        heights = jax.random.uniform(jax.random.fold_in(jax.random.fold_in(rng, 6), axis_at), (blocks,), jnp.float32, smallest / len(shards), high / len(shards))
        return jnp.repeat(jnp.exp(heights), extent[axis_at] // blocks).reshape((-1,) + (1,) * (len(extent) - axis_at - 1))

    gain = one(*shards[0])
    for cut in shards[1:]:
        gain = gain * one(*cut)
    return gain


def different_ones(key, rows, number_of, top, lift):
    order = jax.random.permutation(jax.random.fold_in(key, 1), number_of)
    pull = order
    for power in range(3):
        pull = pull * pull // number_of
    pull = pull * lift // number_of
    tickets = jax.random.randint(jax.random.fold_in(key, 2), (rows, number_of), 0, 4096) + pull
    holders = jax.random.permutation(jax.random.fold_in(key, 3), rows)[jnp.arange(number_of) % rows]
    tickets = jnp.where(jnp.arange(rows)[:, None] == holders[None, :], 1 << 14, tickets)
    priority = tickets * number_of + jnp.arange(number_of)
    return lax.top_k(priority.astype(jnp.int32), top)[1].astype(jnp.int32)


def profile(number_of, total, reach, skew):
    portions = [(1 << 20) // math.isqrt(rank ** skew) + 1 for rank in range(2, number_of + 1)]
    surplus, counts = total - reach - (number_of - 1), [1] * (number_of - 1)
    while surplus > 0:
        candidates = [i for i in range(number_of - 1) if counts[i] < reach]
        whole, remaining = sum([portions[i] for i in candidates]), surplus
        for i in candidates:
            extra = min(reach - counts[i], max(1, remaining * portions[i] // whole), surplus)
            counts[i] = counts[i] + extra
            surplus = surplus - extra
    return np.array([reach] + counts)


def uneven(key, number_of, total, reach, slope):
    if number_of == 2:
        one = jax.random.randint(key, (), max(1, total - reach), min(reach, total - 1) + 1)
        return jnp.stack([one, total - one])
    tallies = jnp.asarray(profile(number_of, total, reach, slope), jnp.int32)
    twos = (number_of - 1) // 2
    giver, sink = tallies[1:1 + 2 * twos:2], tallies[2:2 + 2 * twos:2]
    slack = jnp.minimum(giver - 1, reach - sink)
    shifted = jax.random.randint(jax.random.fold_in(key, 1), (twos,), 0, 1 << 20) % (slack + 1)
    tallies = tallies.at[1:1 + 2 * twos:2].set(giver - shifted).at[2:2 + 2 * twos:2].set(sink + shifted)
    return tallies[jax.random.permutation(jax.random.fold_in(key, 2), number_of)]


def noise(rng, extent, scale, bound, split=(), kind=jnp.bfloat16):
    values = jax.random.normal(rng, extent, jnp.float32) * scale
    if len(split) > 0:
        values = shard_levels(rng, extent, split, -0.22, 0.18) * values
    return jnp.clip(values, min=-bound, max=bound).astype(kind)


def setup_inputs(seed: int = 0) -> dict:
    splits = jax.random.split(jax.random.key(seed), 7)
    a_vals = noise(splits[0], (N_REP, NB, ASL_DEV, BS, BS), (BS * ASL_DEV) ** -0.5, 0.25, ((0, 4), (1, 64)), jnp.float32)
    a_tgt = different_ones(splits[1], N_REP * NB, TG, ASL_DEV, 0).reshape((N_REP, NB, ASL_DEV))
    b_vals = noise(splits[2], (NB, BS, BSL, BS), 1.0, 6.0, ((0, 256),), jnp.float32)
    b_cols = draw_b_cols(jax.random.fold_in(splits[6], 71), 0)
    c_cols = draw_c_cols(jax.random.fold_in(splits[6], 71), 0)
    c_count = uneven(splits[5], NB, NB * CAVG, CSL, 2).astype(jnp.int32)
    return dict(a_vals=a_vals, a_tgt=a_tgt, b_vals=b_vals, b_cols=b_cols, c_cols=c_cols, c_count=c_count)


highest = lax.Precision.HIGHEST


def group_products(blocks, b_group, targets, target_count):
    chosen = (targets[:, :, None] == jnp.arange(target_count, dtype=jnp.int32)[None, None, :]).astype(jnp.float32)
    products = jnp.einsum('ksab,kbtc->ksatc', blocks, b_group, precision=highest)
    return jnp.einsum('kse,ksatc->eatc', chosen, products, precision=highest)


def reference(a_vals, a_tgt, b_vals, b_cols, c_cols, c_count):
    replicas = a_vals.shape[0]
    groups = b_cols.shape[0]
    total_rows = b_vals.shape[0]
    group_rows = total_rows // groups
    rows_dev = group_rows // replicas
    spread = 2 * REACH + 1
    target_count = spread * rows_dev
    c_slots = c_cols.shape[1]
    block_edge = b_vals.shape[1]
    b_slots = b_vals.shape[2]
    slot_ids = jnp.arange(c_slots, dtype=jnp.int32)
    pattern = jnp.where(slot_ids[None, :] < c_count[:, None], c_cols, -1)

    def add_group(result, group_id):
        b_group = lax.dynamic_slice_in_dim(b_vals, group_id * group_rows, group_rows, 0)
        blocks = lax.dynamic_slice_in_dim(a_vals, group_id * group_rows, group_rows, 1)
        targets = lax.dynamic_slice_in_dim(a_tgt, group_id * group_rows, group_rows, 1)
        columns = lax.dynamic_index_in_dim(b_cols, group_id, 0, keepdims=False)
        partial_value = jnp.stack([group_products(blocks[residue], b_group, targets[residue], target_count) for residue in range(replicas)])
        partial_value = partial_value.reshape(replicas, spread, rows_dev, block_edge, b_slots, block_edge)
        for hop_index in range(spread):
            owner_id = (group_id + hop_index - REACH) % groups
            first_row = owner_id * group_rows
            owner_rows = lax.dynamic_slice_in_dim(pattern, first_row, group_rows, 0).reshape(replicas, rows_dev, c_slots)
            weights = (owner_rows[:, :, :, None] == columns[None, None, None, :]).astype(jnp.float32)
            mapped = jnp.einsum('quct,quatb->qucab', weights, partial_value[:, hop_index], precision=highest)
            mapped = mapped.reshape(group_rows, c_slots, block_edge, block_edge)
            current = lax.dynamic_slice_in_dim(result, first_row, group_rows, 0)
            result = lax.dynamic_update_slice_in_dim(result, current + mapped, first_row, 0)
        return result, None

    starting = jnp.zeros((total_rows, c_slots, block_edge, block_edge), jnp.float32)
    c_vals, _ = lax.scan(add_group, starting, jnp.arange(groups, dtype=jnp.int32))
    row_start = jnp.cumsum(c_count, dtype=jnp.int32) - c_count
    return c_vals, row_start
```

```python
import jax
import jax.numpy as jnp
from jax import lax
from jax.sharding import PartitionSpec as P

REACH = 2


highest = lax.Precision.HIGHEST


def shifted(value, axis, by):
    size = lax.axis_size(axis)
    return lax.ppermute(value, axis, [(i, (i + by) % size) for i in range(size)])


def carried_in(part, axis, combine, identity):
    place = lax.axis_index(axis)
    gathered = lax.all_gather(part, axis)
    state = jnp.zeros_like(part) + jnp.asarray(identity, part.dtype)

    def one(lap, state):
        return combine(state, lax.dynamic_index_in_dim(gathered, lap, 0, False))

    return lax.fori_loop(0, place, one, state)


def target_matrix(targets, target_count):
    return (targets[:, :, None] == jnp.arange(target_count, dtype=jnp.int32)[None, None, :]).astype(
        jnp.float32
    )


def add_counts(former, latter):
    return former + latter


def local(a_vals, a_tgt, b_vals, b_cols, c_cols, c_count):
    blocks = a_vals[0]
    targets = a_tgt[0]
    rows_dev = b_vals.shape[0]
    block_edge = b_vals.shape[1]
    b_slots = b_vals.shape[2]
    a_slots = blocks.shape[1]
    spread = 2 * REACH + 1
    target_count = spread * rows_dev
    b_piece = lax.all_gather(b_vals, "rep", axis=0, tiled=True)
    k_count = b_piece.shape[0]
    a_part = blocks.reshape(k_count, a_slots * block_edge, block_edge)
    chosen = target_matrix(targets, target_count)
    b_part = b_piece.reshape(k_count, block_edge, b_slots * block_edge)
    products = lax.dot_general(
        a_part,
        b_part,
        (((2,), (1,)), ((0,), (0,))),
        precision=highest,
        preferred_element_type=jnp.float32,
    )
    products = products.reshape(k_count, a_slots, block_edge, b_slots * block_edge)
    partial_value = jnp.einsum("kse,ksaj->eaj", chosen, products, precision=highest)
    partial_value = partial_value.reshape(spread, rows_dev, block_edge, b_slots, block_edge)
    own_cols = b_cols[0]
    slot_ids = jnp.arange(c_cols.shape[1], dtype=jnp.int32)
    pattern = jnp.where(slot_ids[None, :] < c_count[:, None], c_cols, -1)
    col_tags = own_cols.astype(jnp.float32)
    arrived = []
    sender_cols = []
    for hop_index in range(spread):
        shift_by = hop_index - REACH
        if shift_by == 0:
            arrived.append(partial_value[hop_index])
            sender_cols.append(own_cols)
        else:
            moved, moved_tags = shifted((partial_value[hop_index], col_tags), "rows", shift_by)
            arrived.append(moved)
            sender_cols.append(moved_tags.astype(jnp.int32))
    arrived = jnp.stack(arrived)
    sender_cols = jnp.stack(sender_cols)
    weights = (pattern[:, :, None, None] == sender_cols[None, None, :, :]).astype(jnp.float32)
    result = jnp.einsum("ucdt,duatb->ucab", weights, arrived, precision=highest)
    before = jnp.cumsum(c_count, dtype=jnp.int32) - c_count
    all_counts = lax.all_gather(c_count, ("rows", "rep"), axis=0, tiled=True)
    first_row = lax.axis_index(("rows", "rep")) * c_count.shape[0]
    row_ids = jnp.arange(all_counts.shape[0], dtype=jnp.int32)
    earlier = jnp.sum(jnp.where(row_ids < first_row, all_counts, 0))
    row_start = earlier + before
    return (result, row_start)


def solution(mesh):
    in_specs = (
        P("rep", "rows", None, None, None),
        P("rep", "rows", None),
        P(("rows", "rep"), None, None, None),
        P("rows", None),
        P(("rows", "rep"), None),
        P(("rows", "rep")),
    )
    out_specs = (P(("rows", "rep"), None, None, None), P(("rows", "rep")))
    return jax.shard_map(local, mesh=mesh, in_specs=in_specs, out_specs=out_specs, check_vma=False)
```

```python
import jax
import jax.numpy as jnp
from jax import lax
from jax.sharding import PartitionSpec as P

REACH = 2
COUNT_PAD = 1024

highest = lax.Precision.HIGHEST
high = lax.Precision.HIGH


def shifted(value, axis, by):
    size = lax.axis_size(axis)
    return lax.ppermute(value, axis, [(i, (i + by) % size) for i in range(size)])


def earlier_counts(c_count):
    padded = jnp.zeros((COUNT_PAD,), jnp.int32).at[: c_count.shape[0]].set(c_count)
    gathered = lax.all_gather(padded, ("rows", "rep"), axis=0)
    all_counts = gathered[:, : c_count.shape[0]].reshape(-1)
    first_row = lax.axis_index(("rows", "rep")) * c_count.shape[0]
    row_ids = jnp.arange(all_counts.shape[0], dtype=jnp.int32)
    return jnp.sum(jnp.where(row_ids < first_row, all_counts, 0))


def local(a_vals, a_tgt, b_vals, b_cols, c_cols, c_count):
    blocks = a_vals[0]
    targets = a_tgt[0]
    rows_dev = b_vals.shape[0]
    block_edge = b_vals.shape[1]
    b_slots = b_vals.shape[2]
    k_count = blocks.shape[0]
    spread = 2 * REACH + 1
    target_count = spread * rows_dev
    n_rep = lax.axis_size("rep")
    place = lax.axis_index("rep")

    hit = targets[None, :, :] == jnp.arange(target_count, dtype=jnp.int32)[:, None, None]
    selected = jnp.sum(jnp.where(hit[:, :, :, None, None], blocks[None], 0.0), axis=2)

    def chunk_product(b_chunk, source):
        a_chunk = lax.dynamic_slice_in_dim(selected, source * rows_dev, rows_dev, 1)
        b_flat = b_chunk.reshape(rows_dev, block_edge, b_slots * block_edge)
        return lax.dot_general(
            a_chunk,
            b_flat,
            (((1, 3), (0, 1)), ((), ())),
            precision=high,
            preferred_element_type=jnp.float32,
        )

    partial_value = chunk_product(b_vals, place)
    for by in range(1, n_rep):
        arrived_b = shifted(b_vals, "rep", by)
        partial_value = partial_value + chunk_product(arrived_b, (place - by) % n_rep)
    partial_value = partial_value.reshape(spread, rows_dev, block_edge, b_slots, block_edge)

    own_cols = b_cols[0]
    slot_ids = jnp.arange(c_cols.shape[1], dtype=jnp.int32)
    pattern = jnp.where(slot_ids[None, :] < c_count[:, None], c_cols, -1)
    col_tags = own_cols.astype(jnp.float32)
    arrived = []
    sender_cols = []
    for hop_index in range(spread):
        shift_by = hop_index - REACH
        if shift_by == 0:
            arrived.append(partial_value[hop_index])
            sender_cols.append(own_cols)
        else:
            moved, moved_tags = shifted((partial_value[hop_index], col_tags), "rows", shift_by)
            arrived.append(moved)
            sender_cols.append(moved_tags.astype(jnp.int32))
    arrived = jnp.stack(arrived)
    sender_cols = jnp.stack(sender_cols)
    weights = (pattern[:, :, None, None] == sender_cols[None, None, :, :]).astype(jnp.float32)
    result = jnp.einsum("ucdt,duatb->ucab", weights, arrived, precision=highest)
    before = jnp.cumsum(c_count, dtype=jnp.int32) - c_count
    row_start = earlier_counts(c_count) + before
    return (result, row_start)


def solution(mesh):
    in_specs = (
        P("rep", "rows", None, None, None),
        P("rep", "rows", None),
        P(("rows", "rep"), None, None, None),
        P("rows", None),
        P(("rows", "rep"), None),
        P(("rows", "rep")),
    )
    out_specs = (P(("rows", "rep"), None, None, None), P(("rows", "rep")))
    return jax.shard_map(local, mesh=mesh, in_specs=in_specs, out_specs=out_specs, check_vma=False)
```

```python
import jax
import jax.numpy as jnp
from jax import lax
from jax.sharding import PartitionSpec as P

REACH = 2
COUNT_PAD = 1024

highest = lax.Precision.HIGHEST
high = lax.Precision.HIGH


def shifted(value, axis, by):
    size = lax.axis_size(axis)
    return lax.ppermute(value, axis, [(i, (i + by) % size) for i in range(size)])


def earlier_counts(c_count):
    padded = jnp.zeros((COUNT_PAD,), jnp.int32).at[: c_count.shape[0]].set(c_count)
    gathered = lax.all_gather(padded, ("rows", "rep"), axis=0)
    all_counts = gathered[:, : c_count.shape[0]].reshape(-1)
    first_row = lax.axis_index(("rows", "rep")) * c_count.shape[0]
    row_ids = jnp.arange(all_counts.shape[0], dtype=jnp.int32)
    return jnp.sum(jnp.where(row_ids < first_row, all_counts, 0))


def local(a_vals, a_tgt, b_vals, b_cols, c_cols, c_count):
    blocks = a_vals[0]
    targets = a_tgt[0]
    rows_dev = b_vals.shape[0]
    block_edge = b_vals.shape[1]
    b_slots = b_vals.shape[2]
    k_count = blocks.shape[0]
    spread = 2 * REACH + 1
    target_count = spread * rows_dev
    n_rep = lax.axis_size("rep")
    place = lax.axis_index("rep")

    hit = targets[None, :, :] == jnp.arange(target_count, dtype=jnp.int32)[:, None, None]
    selected = jnp.sum(jnp.where(hit[:, :, :, None, None], blocks[None], 0.0), axis=2)

    def chunk_product(b_chunk, source):
        a_chunk = lax.dynamic_slice_in_dim(selected, source * rows_dev, rows_dev, 1)
        b_flat = b_chunk.reshape(rows_dev, block_edge, b_slots * block_edge)
        return lax.dot_general(
            a_chunk,
            b_flat,
            (((1, 3), (0, 1)), ((), ())),
            precision=high,
            preferred_element_type=jnp.float32,
        )

    partial_value = chunk_product(b_vals, place)
    for by in range(1, n_rep):
        arrived_b = shifted(b_vals, "rep", by)
        partial_value = partial_value + chunk_product(arrived_b, (place - by) % n_rep)
    partial_value = partial_value.reshape(spread, rows_dev, block_edge, b_slots, block_edge)

    own_cols = b_cols[0]
    slot_ids = jnp.arange(c_cols.shape[1], dtype=jnp.int32)
    pattern = jnp.where(slot_ids[None, :] < c_count[:, None], c_cols, -1)
    wanted = []
    for hop_index in range(spread):
        shift_by = hop_index - REACH
        wanted.append(pattern if shift_by == 0 else shifted(pattern, "rows", -shift_by))
    wanted = jnp.stack(wanted).reshape(spread, rows_dev, c_cols.shape[1])
    weights = (wanted[:, :, :, None] == own_cols[None, None, None, :]).astype(jnp.float32)
    mapped = jnp.einsum("huct,huatb->hucab", weights, partial_value, precision=highest)
    result = mapped[REACH]
    for shift_by in (2, -2, 1, -1):
        result = result + shifted(mapped[shift_by + REACH], "rows", shift_by)
    before = jnp.cumsum(c_count, dtype=jnp.int32) - c_count
    row_start = earlier_counts(c_count) + before
    return (result, row_start)


def solution(mesh):
    in_specs = (
        P("rep", "rows", None, None, None),
        P("rep", "rows", None),
        P(("rows", "rep"), None, None, None),
        P("rows", None),
        P(("rows", "rep"), None),
        P(("rows", "rep")),
    )
    out_specs = (P(("rows", "rep"), None, None, None), P(("rows", "rep")))
    return jax.shard_map(local, mesh=mesh, in_specs=in_specs, out_specs=out_specs, check_vma=False)
```

```python
import jax
import jax.numpy as jnp
from jax import lax
from jax.sharding import PartitionSpec as P

REACH = 2
COUNT_PAD = 1024


highest = lax.Precision.HIGHEST
high = lax.Precision.HIGH


def shifted(value, axis, by):
    size = lax.axis_size(axis)
    return lax.ppermute(value, axis, [(i, (i + by) % size) for i in range(size)])


def earlier_counts(c_count):
    padded = jnp.zeros((COUNT_PAD,), jnp.int32).at[: c_count.shape[0]].set(c_count)
    gathered = lax.all_gather(padded, ("rows", "rep"), axis=0)
    all_counts = gathered[:, : c_count.shape[0]].reshape(-1)
    first_row = lax.axis_index(("rows", "rep")) * c_count.shape[0]
    row_ids = jnp.arange(all_counts.shape[0], dtype=jnp.int32)
    return jnp.sum(jnp.where(row_ids < first_row, all_counts, 0))


def local(a_vals, a_tgt, b_vals, b_cols, c_cols, c_count):
    blocks = a_vals[0]
    targets = a_tgt[0]
    rows_dev = b_vals.shape[0]
    block_edge = b_vals.shape[1]
    b_slots = b_vals.shape[2]
    k_count = blocks.shape[0]
    spread = 2 * REACH + 1
    target_count = spread * rows_dev
    n_rep = lax.axis_size("rep")
    place = lax.axis_index("rep")

    hit = targets[None, :, :] == jnp.arange(target_count, dtype=jnp.int32)[:, None, None]
    selected = jnp.sum(jnp.where(hit[:, :, :, None, None], blocks[None], 0.0), axis=2)

    def chunk_product(b_chunk, source):
        a_chunk = lax.dynamic_slice_in_dim(selected, source * rows_dev, rows_dev, 1)
        b_flat = b_chunk.reshape(rows_dev, block_edge, b_slots * block_edge)
        return lax.dot_general(
            a_chunk,
            b_flat,
            (((1, 3), (0, 1)), ((), ())),
            precision=high,
            preferred_element_type=jnp.float32,
        )

    partial_value = chunk_product(b_vals, place)
    for by in range(1, n_rep):
        arrived_b = shifted(b_vals, "rep", by)
        partial_value = partial_value + chunk_product(arrived_b, (place - by) % n_rep)

    own_cols = b_cols[0]
    c_slots = c_cols.shape[1]
    slot_ids = jnp.arange(c_slots, dtype=jnp.int32)
    pattern = jnp.where(slot_ids[None, :] < c_count[:, None], c_cols, -1)
    wanted = []
    for hop_index in range(spread):
        shift_by = hop_index - REACH
        wanted.append(pattern if shift_by == 0 else shifted(pattern, "rows", -shift_by))
    wanted = jnp.stack(wanted).reshape(target_count, c_slots)
    match = wanted[:, :, None] == own_cols[None, None, :]
    pieces = [partial_value[:, :, t * block_edge : (t + 1) * block_edge] for t in range(b_slots)]
    kept = []
    for slot in range(c_slots):
        acc = jnp.where(match[:, slot, 0][:, None, None], pieces[0], 0.0)
        for t in range(1, b_slots):
            acc = acc + jnp.where(match[:, slot, t][:, None, None], pieces[t], 0.0)
        kept.append(acc)
    mapped = jnp.concatenate(kept, axis=2).reshape(spread, rows_dev, block_edge, c_slots * block_edge)
    result = mapped[REACH]
    for shift_by in (2, -2, 1, -1):
        result = result + shifted(mapped[shift_by + REACH], "rows", shift_by)
    result = jnp.transpose(result.reshape(rows_dev, block_edge, c_slots, block_edge), (0, 2, 1, 3))
    before = jnp.cumsum(c_count, dtype=jnp.int32) - c_count
    row_start = earlier_counts(c_count) + before
    return (result, row_start)


def solution(mesh):
    in_specs = (
        P("rep", "rows", None, None, None),
        P("rep", "rows", None),
        P(("rows", "rep"), None, None, None),
        P("rows", None),
        P(("rows", "rep"), None),
        P(("rows", "rep")),
    )
    out_specs = (P(("rows", "rep"), None, None, None), P(("rows", "rep")))
    return jax.shard_map(local, mesh=mesh, in_specs=in_specs, out_specs=out_specs, check_vma=False)
```

```python
import jax
import jax.numpy as jnp
from jax import lax
from jax.sharding import PartitionSpec as P

REACH = 2
COUNT_PAD = 1024


highest = lax.Precision.HIGHEST
high = lax.Precision.HIGH


def shifted(value, axis, by):
    size = lax.axis_size(axis)
    return lax.ppermute(value, axis, [(i, (i + by) % size) for i in range(size)])


def earlier_counts(c_count):
    padded = jnp.zeros((COUNT_PAD,), jnp.int32).at[: c_count.shape[0]].set(c_count)
    gathered = lax.all_gather(padded, ("rows", "rep"), axis=0)
    all_counts = gathered[:, : c_count.shape[0]].reshape(-1)
    first_row = lax.axis_index(("rows", "rep")) * c_count.shape[0]
    row_ids = jnp.arange(all_counts.shape[0], dtype=jnp.int32)
    return jnp.sum(jnp.where(row_ids < first_row, all_counts, 0))


def local(a_vals, a_tgt, b_vals, b_cols, c_cols, c_count):
    blocks = a_vals[0]
    targets = a_tgt[0]
    rows_dev = b_vals.shape[0]
    block_edge = b_vals.shape[1]
    b_slots = b_vals.shape[2]
    k_count = blocks.shape[0]
    spread = 2 * REACH + 1
    target_count = spread * rows_dev
    n_rep = lax.axis_size("rep")
    place = lax.axis_index("rep")

    hit = targets[None, :, :] == jnp.arange(target_count, dtype=jnp.int32)[:, None, None]
    selected = jnp.sum(jnp.where(hit[:, :, :, None, None], blocks[None], 0.0), axis=2)

    def rows_product(b_rows, first_k):
        a_chunk = lax.dynamic_slice_in_dim(selected, first_k, b_rows.shape[0], 1)
        b_flat = b_rows.reshape(b_rows.shape[0], block_edge, b_slots * block_edge)
        return lax.dot_general(
            a_chunk,
            b_flat,
            (((1, 3), (0, 1)), ((), ())),
            precision=high,
            preferred_element_type=jnp.float32,
        )

    partial_value = rows_product(b_vals, place * rows_dev)
    if n_rep == 4 and rows_dev == 2:
        from_left = shifted(b_vals, "rep", 1)
        from_right = shifted(b_vals, "rep", -1)
        far_first = shifted(from_left[:1], "rep", 1)
        far_second = shifted(from_right[1:], "rep", -1)
        partial_value = partial_value + rows_product(from_left, ((place - 1) % n_rep) * rows_dev)
        partial_value = partial_value + rows_product(from_right, ((place + 1) % n_rep) * rows_dev)
        far = jnp.concatenate([far_first, far_second], axis=0)
        partial_value = partial_value + rows_product(far, ((place + 2) % n_rep) * rows_dev)
    else:
        for by in range(1, n_rep):
            arrived_b = shifted(b_vals, "rep", by)
            partial_value = partial_value + rows_product(arrived_b, ((place - by) % n_rep) * rows_dev)

    own_cols = b_cols[0]
    c_slots = c_cols.shape[1]
    slot_ids = jnp.arange(c_slots, dtype=jnp.int32)
    pattern = jnp.where(slot_ids[None, :] < c_count[:, None], c_cols, -1)
    wanted = []
    for hop_index in range(spread):
        shift_by = hop_index - REACH
        wanted.append(pattern if shift_by == 0 else shifted(pattern, "rows", -shift_by))
    wanted = jnp.stack(wanted).reshape(target_count, c_slots)
    match = wanted[:, :, None] == own_cols[None, None, :]
    pieces = [partial_value[:, :, t * block_edge : (t + 1) * block_edge] for t in range(b_slots)]
    kept = []
    for slot in range(c_slots):
        acc = jnp.where(match[:, slot, 0][:, None, None], pieces[0], 0.0)
        for t in range(1, b_slots):
            acc = acc + jnp.where(match[:, slot, t][:, None, None], pieces[t], 0.0)
        kept.append(acc)
    mapped = jnp.concatenate(kept, axis=2).reshape(spread, rows_dev, block_edge, c_slots * block_edge)
    result = mapped[REACH]
    for shift_by in (2, -2, 1, -1):
        result = result + shifted(mapped[shift_by + REACH], "rows", shift_by)
    result = jnp.transpose(result.reshape(rows_dev, block_edge, c_slots, block_edge), (0, 2, 1, 3))
    before = jnp.cumsum(c_count, dtype=jnp.int32) - c_count
    row_start = earlier_counts(c_count) + before
    return (result, row_start)


def solution(mesh):
    in_specs = (
        P("rep", "rows", None, None, None),
        P("rep", "rows", None),
        P(("rows", "rep"), None, None, None),
        P("rows", None),
        P(("rows", "rep"), None),
        P(("rows", "rep")),
    )
    out_specs = (P(("rows", "rep"), None, None, None), P(("rows", "rep")))
    return jax.shard_map(local, mesh=mesh, in_specs=in_specs, out_specs=out_specs, check_vma=False)
```

```python
import jax
import jax.numpy as jnp
from jax import lax
from jax.sharding import PartitionSpec as P

REACH = 2


highest = lax.Precision.HIGHEST
high = lax.Precision.HIGH


def shifted(value, axis, by):
    size = lax.axis_size(axis)
    return lax.ppermute(value, axis, [(i, (i + by) % size) for i in range(size)])


def earlier_counts(total, axes, size):
    running = total
    by = 1
    while by < size:
        running = running + lax.ppermute(running, axes, [(i, i + by) for i in range(size - by)])
        by *= 2
    return running - total


def local(a_vals, a_tgt, b_vals, b_cols, c_cols, c_count):
    blocks = a_vals[0]
    targets = a_tgt[0]
    rows_dev = b_vals.shape[0]
    block_edge = b_vals.shape[1]
    b_slots = b_vals.shape[2]
    k_count = blocks.shape[0]
    spread = 2 * REACH + 1
    target_count = spread * rows_dev
    n_rep = lax.axis_size("rep")
    place = lax.axis_index("rep")

    hit = targets[None, :, :] == jnp.arange(target_count, dtype=jnp.int32)[:, None, None]
    selected = jnp.sum(jnp.where(hit[:, :, :, None, None], blocks[None], 0.0), axis=2)

    def rows_product(b_rows, first_k):
        a_chunk = lax.dynamic_slice_in_dim(selected, first_k, b_rows.shape[0], 1)
        b_flat = b_rows.reshape(b_rows.shape[0], block_edge, b_slots * block_edge)
        return lax.dot_general(
            a_chunk,
            b_flat,
            (((1, 3), (0, 1)), ((), ())),
            precision=high,
            preferred_element_type=jnp.float32,
        )

    partial_value = rows_product(b_vals, place * rows_dev)
    if n_rep == 4 and rows_dev == 2:
        from_left = shifted(b_vals, "rep", 1)
        from_right = shifted(b_vals, "rep", -1)
        from_left, c_cols, c_count = lax.optimization_barrier((from_left, c_cols, c_count))
        far_first = shifted(from_left[:1], "rep", 1)
        far_second = shifted(from_right[1:], "rep", -1)
        partial_value = partial_value + rows_product(from_left, ((place - 1) % n_rep) * rows_dev)
        partial_value = partial_value + rows_product(from_right, ((place + 1) % n_rep) * rows_dev)
        far = jnp.concatenate([far_first, far_second], axis=0)
        partial_value = partial_value + rows_product(far, ((place + 2) % n_rep) * rows_dev)
    else:
        for by in range(1, n_rep):
            arrived_b = shifted(b_vals, "rep", by)
            partial_value = partial_value + rows_product(arrived_b, ((place - by) % n_rep) * rows_dev)

    own_cols = b_cols[0]
    c_slots = c_cols.shape[1]
    slot_ids = jnp.arange(c_slots, dtype=jnp.int32)
    pattern = jnp.where(slot_ids[None, :] < c_count[:, None], c_cols, -1)
    wanted = []
    for hop_index in range(spread):
        shift_by = hop_index - REACH
        wanted.append(pattern if shift_by == 0 else shifted(pattern, "rows", -shift_by))
    wanted = jnp.stack(wanted).reshape(target_count, c_slots)
    match = wanted[:, :, None] == own_cols[None, None, :]
    pieces = [partial_value[:, :, t * block_edge : (t + 1) * block_edge] for t in range(b_slots)]
    kept = []
    for slot in range(c_slots):
        acc = jnp.where(match[:, slot, 0][:, None, None], pieces[0], 0.0)
        for t in range(1, b_slots):
            acc = acc + jnp.where(match[:, slot, t][:, None, None], pieces[t], 0.0)
        kept.append(acc)
    mapped = jnp.concatenate(kept, axis=2).reshape(spread, rows_dev, block_edge, c_slots * block_edge)
    result = mapped[REACH]
    for shift_by in (2, -2, 1, -1):
        result = result + shifted(mapped[shift_by + REACH], "rows", shift_by)
    result = jnp.transpose(result.reshape(rows_dev, block_edge, c_slots, block_edge), (0, 2, 1, 3))
    before = jnp.cumsum(c_count, dtype=jnp.int32) - c_count
    n_dev = lax.axis_size("rows") * n_rep
    earlier = earlier_counts(jnp.sum(c_count).reshape(1), ("rows", "rep"), n_dev)
    row_start = earlier + before
    return (result, row_start)


def solution(mesh):
    in_specs = (
        P("rep", "rows", None, None, None),
        P("rep", "rows", None),
        P(("rows", "rep"), None, None, None),
        P("rows", None),
        P(("rows", "rep"), None),
        P(("rows", "rep")),
    )
    out_specs = (P(("rows", "rep"), None, None, None), P(("rows", "rep")))
    return jax.shard_map(local, mesh=mesh, in_specs=in_specs, out_specs=out_specs, check_vma=False)
```

```python
import jax
import jax.numpy as jnp
from jax import lax
from jax.sharding import PartitionSpec as P

REACH = 2
COUNT_PAD = 1024


highest = lax.Precision.HIGHEST
high = lax.Precision.HIGH


def shifted(value, axis, by):
    size = lax.axis_size(axis)
    return lax.ppermute(value, axis, [(i, (i + by) % size) for i in range(size)])


def earlier_counts(c_count):
    padded = jnp.zeros((COUNT_PAD,), jnp.int32).at[: c_count.shape[0]].set(c_count)
    gathered = lax.all_gather(padded, ("rows", "rep"), axis=0)
    all_counts = gathered[:, : c_count.shape[0]].reshape(-1)
    first_row = lax.axis_index(("rows", "rep")) * c_count.shape[0]
    row_ids = jnp.arange(all_counts.shape[0], dtype=jnp.int32)
    return jnp.sum(jnp.where(row_ids < first_row, all_counts, 0))


def local(a_vals, a_tgt, b_vals, b_cols, c_cols, c_count):
    blocks = a_vals[0]
    targets = a_tgt[0]
    rows_dev = b_vals.shape[0]
    block_edge = b_vals.shape[1]
    b_slots = b_vals.shape[2]
    k_count = blocks.shape[0]
    spread = 2 * REACH + 1
    target_count = spread * rows_dev
    n_rep = lax.axis_size("rep")
    place = lax.axis_index("rep")

    hit = targets[None, :, :] == jnp.arange(target_count, dtype=jnp.int32)[:, None, None]
    selected = jnp.sum(jnp.where(hit[:, :, :, None, None], blocks[None], 0.0), axis=2)

    def rows_product(b_rows, first_k, targets_from=0, targets=target_count):
        a_chunk = lax.dynamic_slice_in_dim(selected, first_k, b_rows.shape[0], 1)[targets_from : targets_from + targets]
        b_flat = b_rows.reshape(b_rows.shape[0], block_edge, b_slots * block_edge)
        return lax.dot_general(
            a_chunk,
            b_flat,
            (((1, 3), (0, 1)), ((), ())),
            precision=high,
            preferred_element_type=jnp.float32,
        )

    partial_value = rows_product(b_vals, place * rows_dev)
    far = None
    if n_rep == 4 and rows_dev == 2:
        from_left = shifted(b_vals, "rep", 1)
        from_right = shifted(b_vals, "rep", -1)
        far_first = shifted(from_left[:1], "rep", 1)
        far_second = shifted(from_right[1:], "rep", -1)
        partial_value = partial_value + rows_product(from_left, ((place - 1) % n_rep) * rows_dev)
        partial_value = partial_value + rows_product(from_right, ((place + 1) % n_rep) * rows_dev)
        far = jnp.concatenate([far_first, far_second], axis=0)
        far_k = ((place + 2) % n_rep) * rows_dev
    else:
        for by in range(1, n_rep):
            arrived_b = shifted(b_vals, "rep", by)
            partial_value = partial_value + rows_product(arrived_b, ((place - by) % n_rep) * rows_dev)

    own_cols = b_cols[0]
    c_slots = c_cols.shape[1]
    slot_ids = jnp.arange(c_slots, dtype=jnp.int32)
    pattern = jnp.where(slot_ids[None, :] < c_count[:, None], c_cols, -1)
    wanted = []
    for hop_index in range(spread):
        shift_by = hop_index - REACH
        wanted.append(pattern if shift_by == 0 else shifted(pattern, "rows", -shift_by))
    wanted = jnp.stack(wanted).reshape(target_count, c_slots)
    match = wanted[:, :, None] == own_cols[None, None, :]

    def kept_blocks(hop_value, hop_match):
        pieces = [hop_value[:, :, t * block_edge : (t + 1) * block_edge] for t in range(b_slots)]
        kept = []
        for slot in range(c_slots):
            acc = jnp.where(hop_match[:, slot, 0][:, None, None], pieces[0], 0.0)
            for t in range(1, b_slots):
                acc = acc + jnp.where(hop_match[:, slot, t][:, None, None], pieces[t], 0.0)
            kept.append(acc)
        return jnp.concatenate(kept, axis=2)

    def hop_blocks(hop_index):
        first = hop_index * rows_dev
        hop_value = partial_value[first : first + rows_dev]
        if far is not None:
            hop_value = hop_value + rows_product(far, far_k, first, rows_dev)
        return kept_blocks(hop_value, match[first : first + rows_dev])

    result = None
    for shift_by in (2, -2, 1, -1, 0):
        blocks_out = hop_blocks(shift_by + REACH)
        moved = blocks_out if shift_by == 0 else shifted(blocks_out, "rows", shift_by)
        result = moved if result is None else result + moved
    result = jnp.transpose(result.reshape(rows_dev, block_edge, c_slots, block_edge), (0, 2, 1, 3))
    before = jnp.cumsum(c_count, dtype=jnp.int32) - c_count
    row_start = earlier_counts(c_count) + before
    return (result, row_start)


def solution(mesh):
    in_specs = (
        P("rep", "rows", None, None, None),
        P("rep", "rows", None),
        P(("rows", "rep"), None, None, None),
        P("rows", None),
        P(("rows", "rep"), None),
        P(("rows", "rep")),
    )
    out_specs = (P(("rows", "rep"), None, None, None), P(("rows", "rep")))
    return jax.shard_map(local, mesh=mesh, in_specs=in_specs, out_specs=out_specs, check_vma=False)
```

```python
import jax
import jax.numpy as jnp
from jax import lax
from jax.sharding import PartitionSpec as P

REACH = 2
COUNT_PAD = 1024


highest = lax.Precision.HIGHEST
high = lax.Precision.HIGH


def shifted(value, axis, by):
    size = lax.axis_size(axis)
    return lax.ppermute(value, axis, [(i, (i + by) % size) for i in range(size)])


def earlier_counts(c_count):
    padded = jnp.zeros((COUNT_PAD,), jnp.int32).at[: c_count.shape[0]].set(c_count)
    gathered = lax.all_gather(padded, ("rows", "rep"), axis=0)
    all_counts = gathered[:, : c_count.shape[0]].reshape(-1)
    first_row = lax.axis_index(("rows", "rep")) * c_count.shape[0]
    row_ids = jnp.arange(all_counts.shape[0], dtype=jnp.int32)
    return jnp.sum(jnp.where(row_ids < first_row, all_counts, 0))


def local(a_vals, a_tgt, b_vals, b_cols, c_cols, c_count):
    blocks = a_vals[0]
    targets = a_tgt[0]
    rows_dev = b_vals.shape[0]
    block_edge = b_vals.shape[1]
    b_slots = b_vals.shape[2]
    k_count = blocks.shape[0]
    spread = 2 * REACH + 1
    target_count = spread * rows_dev
    n_rep = lax.axis_size("rep")
    place = lax.axis_index("rep")

    hit = targets[None, :, :] == jnp.arange(target_count, dtype=jnp.int32)[:, None, None]
    selected = jnp.sum(jnp.where(hit[:, :, :, None, None], blocks[None], 0.0), axis=2)

    def rows_product(b_rows, first_k):
        a_chunk = lax.dynamic_slice_in_dim(selected, first_k, b_rows.shape[0], 1)
        b_flat = b_rows.reshape(b_rows.shape[0], block_edge, b_slots * block_edge)
        return lax.dot_general(
            a_chunk,
            b_flat,
            (((1, 3), (0, 1)), ((), ())),
            precision=high,
            preferred_element_type=jnp.float32,
        )

    partial_value = rows_product(b_vals, place * rows_dev)
    if n_rep == 4 and rows_dev == 2:
        left_first = shifted(b_vals[:1], "rep", 1)
        right_second = shifted(b_vals[1:], "rep", -1)
        far_first = shifted(left_first, "rep", 1)
        far_second = shifted(right_second, "rep", -1)
        left_second = shifted(b_vals[1:], "rep", 1)
        right_first = shifted(b_vals[:1], "rep", -1)
        from_left = jnp.concatenate([left_first, left_second], axis=0)
        from_right = jnp.concatenate([right_first, right_second], axis=0)
        partial_value = lax.optimization_barrier(partial_value + rows_product(from_left, ((place - 1) % n_rep) * rows_dev))
        partial_value = lax.optimization_barrier(partial_value + rows_product(from_right, ((place + 1) % n_rep) * rows_dev))
        far = jnp.concatenate([far_first, far_second], axis=0)
        partial_value = partial_value + rows_product(far, ((place + 2) % n_rep) * rows_dev)
    else:
        for by in range(1, n_rep):
            arrived_b = shifted(b_vals, "rep", by)
            partial_value = partial_value + rows_product(arrived_b, ((place - by) % n_rep) * rows_dev)

    own_cols = b_cols[0]
    c_slots = c_cols.shape[1]
    slot_ids = jnp.arange(c_slots, dtype=jnp.int32)
    pattern = jnp.where(slot_ids[None, :] < c_count[:, None], c_cols, -1)
    wanted = []
    for hop_index in range(spread):
        shift_by = hop_index - REACH
        wanted.append(pattern if shift_by == 0 else shifted(pattern, "rows", -shift_by))
    wanted = jnp.stack(wanted).reshape(target_count, c_slots)
    match = wanted[:, :, None] == own_cols[None, None, :]
    pieces = [partial_value[:, :, t * block_edge : (t + 1) * block_edge] for t in range(b_slots)]
    kept = []
    for slot in range(c_slots):
        acc = jnp.where(match[:, slot, 0][:, None, None], pieces[0], 0.0)
        for t in range(1, b_slots):
            acc = acc + jnp.where(match[:, slot, t][:, None, None], pieces[t], 0.0)
        kept.append(acc)
    mapped = jnp.concatenate(kept, axis=2).reshape(spread, rows_dev, block_edge, c_slots * block_edge)
    result = mapped[REACH]
    for shift_by in (2, -2, 1, -1):
        result = result + shifted(mapped[shift_by + REACH], "rows", shift_by)
    result = jnp.transpose(result.reshape(rows_dev, block_edge, c_slots, block_edge), (0, 2, 1, 3))
    before = jnp.cumsum(c_count, dtype=jnp.int32) - c_count
    row_start = earlier_counts(c_count) + before
    return (result, row_start)


def solution(mesh):
    in_specs = (
        P("rep", "rows", None, None, None),
        P("rep", "rows", None),
        P(("rows", "rep"), None, None, None),
        P("rows", None),
        P(("rows", "rep"), None),
        P(("rows", "rep")),
    )
    out_specs = (P(("rows", "rep"), None, None, None), P(("rows", "rep")))
    return jax.shard_map(local, mesh=mesh, in_specs=in_specs, out_specs=out_specs, check_vma=False)
```

```python
import jax
import jax.numpy as jnp
from jax import lax
from jax.sharding import PartitionSpec as P

REACH = 2
COUNT_PAD = 1024


highest = lax.Precision.HIGHEST
high = lax.Precision.HIGH


def shifted(value, axis, by):
    size = lax.axis_size(axis)
    return lax.ppermute(value, axis, [(i, (i + by) % size) for i in range(size)])


def earlier_counts(c_count):
    padded = jnp.zeros((COUNT_PAD,), jnp.int32).at[: c_count.shape[0]].set(c_count)
    gathered = lax.all_gather(padded, ("rows", "rep"), axis=0)
    all_counts = gathered[:, : c_count.shape[0]].reshape(-1)
    first_row = lax.axis_index(("rows", "rep")) * c_count.shape[0]
    row_ids = jnp.arange(all_counts.shape[0], dtype=jnp.int32)
    return jnp.sum(jnp.where(row_ids < first_row, all_counts, 0))


def local(a_vals, a_tgt, b_vals, b_cols, c_cols, c_count):
    blocks = a_vals[0]
    targets = a_tgt[0]
    rows_dev = b_vals.shape[0]
    block_edge = b_vals.shape[1]
    b_slots = b_vals.shape[2]
    k_count = blocks.shape[0]
    spread = 2 * REACH + 1
    target_count = spread * rows_dev
    n_rep = lax.axis_size("rep")
    place = lax.axis_index("rep")

    hit = targets[None, :, :] == jnp.arange(target_count, dtype=jnp.int32)[:, None, None]
    selected = jnp.sum(jnp.where(hit[:, :, :, None, None], blocks[None], 0.0), axis=2)

    def rows_product(b_rows, first_k):
        a_chunk = lax.dynamic_slice_in_dim(selected, first_k, b_rows.shape[0], 1)
        b_flat = b_rows.reshape(b_rows.shape[0], block_edge, b_slots * block_edge)
        return lax.dot_general(
            a_chunk,
            b_flat,
            (((1, 3), (0, 1)), ((), ())),
            precision=high,
            preferred_element_type=jnp.float32,
        )

    partial_value = rows_product(b_vals, place * rows_dev)
    if n_rep == 4 and rows_dev == 2:
        left_first = shifted(b_vals[:1], "rep", 1)
        right_second = shifted(b_vals[1:], "rep", -1)
        far_first = shifted(left_first, "rep", 1)
        far_second = shifted(right_second, "rep", -1)
        left_first, c_cols, pattern_counts = lax.optimization_barrier((left_first, c_cols, c_count))
        left_second = shifted(b_vals[1:], "rep", 1)
        right_first = shifted(b_vals[:1], "rep", -1)
        from_left = jnp.concatenate([left_first, left_second], axis=0)
        from_right = jnp.concatenate([right_first, right_second], axis=0)
        partial_value = lax.optimization_barrier(partial_value + rows_product(from_left, ((place - 1) % n_rep) * rows_dev))
        partial_value = lax.optimization_barrier(partial_value + rows_product(from_right, ((place + 1) % n_rep) * rows_dev))
        far = jnp.concatenate([far_first, far_second], axis=0)
        partial_value = partial_value + rows_product(far, ((place + 2) % n_rep) * rows_dev)
    else:
        for by in range(1, n_rep):
            arrived_b = shifted(b_vals, "rep", by)
            partial_value = partial_value + rows_product(arrived_b, ((place - by) % n_rep) * rows_dev)

    own_cols = b_cols[0]
    c_slots = c_cols.shape[1]
    slot_ids = jnp.arange(c_slots, dtype=jnp.int32)
    pattern = jnp.where(slot_ids[None, :] < pattern_counts[:, None], c_cols, -1)
    wanted = []
    for hop_index in range(spread):
        shift_by = hop_index - REACH
        wanted.append(pattern if shift_by == 0 else shifted(pattern, "rows", -shift_by))
    wanted = jnp.stack(wanted).reshape(target_count, c_slots)
    match = wanted[:, :, None] == own_cols[None, None, :]
    pieces = [partial_value[:, :, t * block_edge : (t + 1) * block_edge] for t in range(b_slots)]
    kept = []
    for slot in range(c_slots):
        acc = jnp.where(match[:, slot, 0][:, None, None], pieces[0], 0.0)
        for t in range(1, b_slots):
            acc = acc + jnp.where(match[:, slot, t][:, None, None], pieces[t], 0.0)
        kept.append(acc)
    mapped = jnp.concatenate(kept, axis=2).reshape(spread, rows_dev, block_edge, c_slots * block_edge)
    result = mapped[REACH]
    for shift_by in (2, -2, 1, -1):
        result = result + shifted(mapped[shift_by + REACH], "rows", shift_by)
    result = jnp.transpose(result.reshape(rows_dev, block_edge, c_slots, block_edge), (0, 2, 1, 3))
    before = jnp.cumsum(c_count, dtype=jnp.int32) - c_count
    row_start = earlier_counts(c_count) + before
    return (result, row_start)


def solution(mesh):
    in_specs = (
        P("rep", "rows", None, None, None),
        P("rep", "rows", None),
        P(("rows", "rep"), None, None, None),
        P("rows", None),
        P(("rows", "rep"), None),
        P(("rows", "rep")),
    )
    out_specs = (P(("rows", "rep"), None, None, None), P(("rows", "rep")))
    return jax.shard_map(local, mesh=mesh, in_specs=in_specs, out_specs=out_specs, check_vma=False)
```

```python
import jax
import jax.numpy as jnp
from jax import lax
from jax.sharding import PartitionSpec as P

REACH = 2
COUNT_PAD = 1024


highest = lax.Precision.HIGHEST
high = lax.Precision.HIGH


def shifted(value, axis, by):
    size = lax.axis_size(axis)
    return lax.ppermute(value, axis, [(i, (i + by) % size) for i in range(size)])


def earlier_counts(c_count):
    padded = jnp.zeros((COUNT_PAD,), jnp.int32).at[: c_count.shape[0]].set(c_count)
    gathered = lax.all_gather(padded, ("rows", "rep"), axis=0)
    all_counts = gathered[:, : c_count.shape[0]].reshape(-1)
    first_row = lax.axis_index(("rows", "rep")) * c_count.shape[0]
    row_ids = jnp.arange(all_counts.shape[0], dtype=jnp.int32)
    return jnp.sum(jnp.where(row_ids < first_row, all_counts, 0))


def local(a_vals, a_tgt, b_vals, b_cols, c_cols, c_count):
    blocks = a_vals[0]
    targets = a_tgt[0]
    rows_dev = b_vals.shape[0]
    block_edge = b_vals.shape[1]
    b_slots = b_vals.shape[2]
    k_count = blocks.shape[0]
    spread = 2 * REACH + 1
    target_count = spread * rows_dev
    n_rep = lax.axis_size("rep")
    place = lax.axis_index("rep")

    hit = targets[None, :, :] == jnp.arange(target_count, dtype=jnp.int32)[:, None, None]
    selected = jnp.sum(jnp.where(hit[:, :, :, None, None], blocks[None], 0.0), axis=2)

    def rows_product(b_rows, first_k):
        a_chunk = lax.dynamic_slice_in_dim(selected, first_k, b_rows.shape[0], 1)
        b_flat = b_rows.reshape(b_rows.shape[0], block_edge, b_slots * block_edge)
        return lax.dot_general(
            a_chunk,
            b_flat,
            (((1, 3), (0, 1)), ((), ())),
            precision=high,
            preferred_element_type=jnp.float32,
        )

    partial_value = rows_product(b_vals, place * rows_dev)
    if n_rep == 4 and rows_dev == 2:
        left_first = shifted(b_vals[:1], "rep", 1)
        right_second = shifted(b_vals[1:], "rep", -1)
        far_first = shifted(left_first, "rep", 1)
        far_second = shifted(right_second, "rep", -1)
        left_second = shifted(b_vals[1:], "rep", 1)
        right_first = shifted(b_vals[:1], "rep", -1)
        from_left = jnp.concatenate([left_first, left_second], axis=0)
        from_right = jnp.concatenate([right_first, right_second], axis=0)
        partial_value = lax.optimization_barrier(partial_value + rows_product(from_left, ((place - 1) % n_rep) * rows_dev))
        partial_value = lax.optimization_barrier(partial_value + rows_product(from_right, ((place + 1) % n_rep) * rows_dev))
        far = jnp.concatenate([far_first, far_second], axis=0)
        partial_value = partial_value + rows_product(far, ((place + 2) % n_rep) * rows_dev)
    else:
        for by in range(1, n_rep):
            arrived_b = shifted(b_vals, "rep", by)
            partial_value = partial_value + rows_product(arrived_b, ((place - by) % n_rep) * rows_dev)

    own_cols = b_cols[0]
    c_slots = c_cols.shape[1]
    slot_ids = jnp.arange(c_slots, dtype=jnp.int32)
    pattern = jnp.where(slot_ids[None, :] < c_count[:, None], c_cols, -1)
    from_next = shifted(pattern, "rows", -1)
    from_prev = shifted(pattern, "rows", 1)
    by_shift = {0: pattern, 1: from_next, -1: from_prev}
    by_shift[2] = shifted(from_next, "rows", -1)
    by_shift[-2] = shifted(from_prev, "rows", 1)
    wanted = [by_shift[hop_index - REACH] for hop_index in range(spread)]
    wanted = jnp.stack(wanted).reshape(target_count, c_slots)
    match = wanted[:, :, None] == own_cols[None, None, :]
    pieces = [partial_value[:, :, t * block_edge : (t + 1) * block_edge] for t in range(b_slots)]
    kept = []
    for slot in range(c_slots):
        acc = jnp.where(match[:, slot, 0][:, None, None], pieces[0], 0.0)
        for t in range(1, b_slots):
            acc = acc + jnp.where(match[:, slot, t][:, None, None], pieces[t], 0.0)
        kept.append(acc)
    mapped = jnp.concatenate(kept, axis=2).reshape(spread, rows_dev, block_edge, c_slots * block_edge)
    result = mapped[REACH]
    for shift_by in (2, -2, 1, -1):
        result = result + shifted(mapped[shift_by + REACH], "rows", shift_by)
    result = jnp.transpose(result.reshape(rows_dev, block_edge, c_slots, block_edge), (0, 2, 1, 3))
    before = jnp.cumsum(c_count, dtype=jnp.int32) - c_count
    row_start = earlier_counts(c_count) + before
    return (result, row_start)


def solution(mesh):
    in_specs = (
        P("rep", "rows", None, None, None),
        P("rep", "rows", None),
        P(("rows", "rep"), None, None, None),
        P("rows", None),
        P(("rows", "rep"), None),
        P(("rows", "rep")),
    )
    out_specs = (P(("rows", "rep"), None, None, None), P(("rows", "rep")))
    return jax.shard_map(local, mesh=mesh, in_specs=in_specs, out_specs=out_specs, check_vma=False)
```
